256 devices in a mesh: seq: 32 (over z, x), grp: 8 (over y, core).
Axes of the slice: x: 4, y: 4, z: 8, core: 2. Of those that a mesh axis runs over, the one named last changes fastest.
Arguments:
- in_gate: bfloat16 [65536, 512], P(('grp', 'seq')), parts along dimension 0, may hold values from -6 to 6
- values: bfloat16 [65536, 512], P(('grp', 'seq')), parts along dimension 0, may hold values from -6 to 6
- out_gate: bfloat16 [65536, 512], P(('grp', 'seq')), parts along dimension 0, may hold values from -6 to 6
- filter_taps: bfloat16 [8192, 512], P('seq'), may hold values from -0.0625 to 0.0625
- skip_gain: float32 [512], replicated, may hold values from -4 to 4
Outputs:
- mixed: bfloat16 [65536, 512], P(('grp', 'seq')), parts along dimension 0
The draws below stay inside these ranges and needn't reach their ends.
There are 8 independent parts, one for each index of `grp`. The reference program is written for one: setup_inputs(seed, part) draws one part's arguments, and reference() takes and returns one part's arrays. A program takes and returns all parts, laid end to end along the dimension named above; an argument that names none is the same for every part. Nothing has to cross between parts.
All inputs are finite; a program needn't handle non-finite values.
Results may differ from the reference program's by a relative error of at most 0.001.
Values sent between devices are 32-bit elements; how exact they have to be, the bound alone decides.
No kernel may reach another device: no remote copies, remote signals or barrier semaphores. Data moves between devices by JAX's collectives and lax.ppermute only.
A program may use at most 64 MiB of HBM per device.

```python
import jax
import jax.numpy as jnp

CH = 512
SEQ_LEN = 8192


def level_of(rng, extent, shards, smallest, largest):
    def one(axis_at, blocks):
        steps = jax.random.uniform(jax.random.fold_in(jax.random.fold_in(rng, 6), axis_at), (blocks,), jnp.float32, smallest / len(shards), largest / len(shards))
        return jnp.repeat(jnp.exp(steps), extent[axis_at] // blocks).reshape((-1,) + (1,) * (len(extent) - axis_at - 1))

    factor_of = one(*shards[0])
    for cut in shards[1:]:
        factor_of = factor_of * one(*cut)
    return factor_of


def noise(key, extent, deviation, reach, pieces=(), dtype=jnp.bfloat16):
    result = deviation * jax.random.normal(key, extent, jnp.float32)
    if pieces:
        result = result * level_of(key, extent, pieces, -0.22, 0.18)
    return jnp.clip(result, -reach, reach).astype(dtype)


def setup_inputs(seed: int = 0, part: int = 0) -> dict:
    streams_of = jax.random.split(jax.random.key(seed), 6)
    own_keys = jax.random.split(jax.random.fold_in(streams_of[5], part), 6)
    return {
        "in_gate": noise(own_keys[0], (SEQ_LEN, CH), 1.0, 6.0, ((0, 32),)),
        "values": noise(own_keys[1], (SEQ_LEN, CH), 1.0, 6.0, ((0, 32),)),
        "out_gate": noise(own_keys[2], (SEQ_LEN, CH), 1.0, 6.0, ((0, 32),)),
        "filter_taps": noise(streams_of[3], (SEQ_LEN, CH), SEQ_LEN ** -0.5, 0.0625, ((0, 32),)),
        "skip_gain": noise(streams_of[4], (CH,), 1.0, 4.0, (), jnp.float32),
    }


def reference(in_gate, values, out_gate, filter_taps, skip_gain):
    gated = in_gate.astype(jnp.float32) * values.astype(jnp.float32)
    taps_real = filter_taps.astype(jnp.float32)
    padded = 2 * SEQ_LEN
    spectrum = jnp.fft.rfft(gated, n=padded, axis=0) * jnp.fft.rfft(taps_real, n=padded, axis=0)
    conv = jnp.fft.irfft(spectrum, n=padded, axis=0)[:SEQ_LEN]
    total = conv + skip_gain[None, :] * gated
    return (out_gate.astype(jnp.float32) * total).astype(jnp.bfloat16)
```

```python
import jax
import jax.numpy as jnp
from jax import lax
from jax.sharding import PartitionSpec as P


def local(in_gate, values, out_gate, filter_taps, skip_gain):
    own_rows, channels = in_gate.shape
    devices = lax.axis_size("seq")
    seq_total = own_rows * devices
    gated = in_gate.astype(jnp.float32) * values.astype(jnp.float32)
    taps = filter_taps.astype(jnp.float32)
    both = jnp.stack([gated, taps])
    spread = lax.all_to_all(both, "seq", split_axis=2, concat_axis=1, tiled=True)
    spread = jnp.swapaxes(spread, 1, 2)
    spectrum = jnp.fft.rfft(spread, n=2 * seq_total, axis=-1)
    conv = jnp.fft.irfft(spectrum[0] * spectrum[1], n=2 * seq_total, axis=-1)[:, :seq_total]
    conv = jnp.swapaxes(conv, 0, 1)
    back = lax.all_to_all(conv, "seq", split_axis=0, concat_axis=1, tiled=True)
    total = back + skip_gain[None, :] * gated
    return (out_gate.astype(jnp.float32) * total).astype(jnp.bfloat16)


def solution(mesh):
    in_specs = (
        P(("grp", "seq"), None),
        P(("grp", "seq"), None),
        P(("grp", "seq"), None),
        P("seq", None),
        P(),
    )
    out_specs = P(("grp", "seq"), None)
    return jax.shard_map(local, mesh=mesh, in_specs=in_specs, out_specs=out_specs, check_vma=False)
```

```python
import jax
import jax.numpy as jnp
from jax import lax
from jax.sharding import PartitionSpec as P

exact_mode = lax.Precision.HIGHEST


def angle_table(rows, cols, period):
    product = jnp.arange(rows, dtype=jnp.int32)[:, None] * jnp.arange(cols, dtype=jnp.int32)[None, :]
    return (product % period).astype(jnp.float32) * (2.0 * jnp.pi / period)


def dft_tables(side, filled):
    first = angle_table(side, filled, side)
    stage_a = jnp.concatenate([jnp.cos(first), -jnp.sin(first)], axis=0)
    second = angle_table(side, side, side)
    cos_b, sin_b = jnp.cos(second), jnp.sin(second)
    forward_b = jnp.block([[cos_b, -sin_b], [sin_b, cos_b]])
    inverse_b = jnp.block([[cos_b, sin_b], [-sin_b, cos_b]])
    twist = angle_table(side, side, side * side)
    return stage_a, forward_b, inverse_b, jnp.cos(twist), jnp.sin(twist)


def causal_conv(signals, taps_count):
    _, ch, n = signals.shape
    side = 128
    filled = n // side
    stage_a, forward_b, inverse_b, twist_cos, twist_sin = dft_tables(side, filled)
    x = signals.reshape(2 * ch, filled, side)
    a = jnp.einsum("kn,bnm->bkm", stage_a, x, precision=exact_mode)
    a_re, a_im = a[:, :side], a[:, side:]
    b_re = a_re * twist_cos + a_im * twist_sin
    b_im = a_im * twist_cos - a_re * twist_sin
    spec = jnp.einsum(
        "bkm,mj->bkj", jnp.concatenate([b_re, b_im], axis=-1), forward_b, precision=exact_mode
    )
    g_re, g_im = spec[:ch, :, :side], spec[:ch, :, side:]
    h_re, h_im = spec[ch:, :, :side], spec[ch:, :, side:]
    prod = jnp.concatenate([g_re * h_re - g_im * h_im, g_re * h_im + g_im * h_re], axis=-1)
    q = jnp.einsum("bkj,jm->bkm", prod, inverse_b, precision=exact_mode)
    q_re, q_im = q[..., :side], q[..., side:]
    r_re = q_re * twist_cos - q_im * twist_sin
    r_im = q_im * twist_cos + q_re * twist_sin
    y = jnp.einsum(
        "kn,bkm->bnm", stage_a, jnp.concatenate([r_re, r_im], axis=1), precision=exact_mode
    )
    return y.reshape(ch, n) * (1.0 / (side * side))


def local(in_gate, values, out_gate, filter_taps, skip_gain):
    gated = in_gate.astype(jnp.float32) * values.astype(jnp.float32)
    taps = filter_taps.astype(jnp.float32)
    both = jnp.stack([gated.T, taps.T])
    spread = lax.all_to_all(both, "seq", split_axis=1, concat_axis=2, tiled=True)
    conv = causal_conv(spread, spread.shape[2])
    back = lax.all_to_all(conv, "seq", split_axis=1, concat_axis=0, tiled=True)
    total = back.T + skip_gain[None, :] * gated
    return (out_gate.astype(jnp.float32) * total).astype(jnp.bfloat16)


def solution(mesh):
    in_specs = (
        P(("grp", "seq"), None),
        P(("grp", "seq"), None),
        P(("grp", "seq"), None),
        P("seq", None),
        P(),
    )
    out_specs = P(("grp", "seq"), None)
    return jax.shard_map(local, mesh=mesh, in_specs=in_specs, out_specs=out_specs, check_vma=False)
```

```python
import jax
import jax.numpy as jnp
from jax import lax
from jax.sharding import PartitionSpec as P

exact_mode = lax.Precision.HIGHEST
SIDE = 128


def angle_table(rows, cols, period):
    product = jnp.arange(rows, dtype=jnp.int32)[:, None] * jnp.arange(cols, dtype=jnp.int32)[None, :]
    return (product % period).astype(jnp.float32) * (2.0 * jnp.pi / period)


def dft_tables(filled):
    first = angle_table(SIDE, filled, SIDE)
    stage_a = jnp.concatenate([jnp.cos(first), -jnp.sin(first)], axis=0)
    second = angle_table(SIDE, SIDE, SIDE)
    cos_b, sin_b = jnp.cos(second), jnp.sin(second)
    forward_b = jnp.block([[cos_b, -sin_b], [sin_b, cos_b]])
    inverse_b = jnp.block([[cos_b, sin_b], [-sin_b, cos_b]])
    twist = angle_table(SIDE, SIDE, SIDE * SIDE)
    return stage_a, forward_b, inverse_b, jnp.cos(twist), jnp.sin(twist)


def spectrum(signal, tables):
    stage_a, forward_b, _, twist_cos, twist_sin = tables
    ch, n = signal.shape
    x = signal.reshape(ch, n // SIDE, SIDE)
    a = jnp.einsum("kn,bnm->bkm", stage_a, x, precision=exact_mode)
    a_re, a_im = a[:, :SIDE], a[:, SIDE:]
    b_re = a_re * twist_cos + a_im * twist_sin
    b_im = a_im * twist_cos - a_re * twist_sin
    return jnp.einsum(
        "bkm,mj->bkj", jnp.concatenate([b_re, b_im], axis=-1), forward_b, precision=exact_mode
    )


def inverse_prefix(spec_g, spec_h, tables, n):
    stage_a, _, inverse_b, twist_cos, twist_sin = tables
    ch = spec_g.shape[0]
    g_re, g_im = spec_g[..., :SIDE], spec_g[..., SIDE:]
    h_re, h_im = spec_h[..., :SIDE], spec_h[..., SIDE:]
    prod = jnp.concatenate([g_re * h_re - g_im * h_im, g_re * h_im + g_im * h_re], axis=-1)
    q = jnp.einsum("bkj,jm->bkm", prod, inverse_b, precision=exact_mode)
    q_re, q_im = q[..., :SIDE], q[..., SIDE:]
    r_re = q_re * twist_cos - q_im * twist_sin
    r_im = q_im * twist_cos + q_re * twist_sin
    y = jnp.einsum(
        "kn,bkm->bnm", stage_a, jnp.concatenate([r_re, r_im], axis=1), precision=exact_mode
    )
    return y.reshape(ch, n) * (1.0 / (SIDE * SIDE))


def local(in_gate, values, out_gate, filter_taps, skip_gain):
    own_rows, channels = in_gate.shape
    copies = lax.axis_size("grp")
    copy_index = lax.axis_index("grp")
    piece = own_rows // copies
    gated = in_gate.astype(jnp.float32) * values.astype(jnp.float32)
    taps_part = lax.dynamic_slice_in_dim(filter_taps, copy_index * piece, piece, axis=0)
    taps_part = taps_part.astype(jnp.float32).T
    taps_spread = lax.all_to_all(taps_part, "seq", split_axis=0, concat_axis=1, tiled=True)
    gated_spread = lax.all_to_all(gated.T, "seq", split_axis=0, concat_axis=1, tiled=True)
    taps_all = lax.all_gather(taps_spread, "grp", axis=0)
    ch = taps_all.shape[1]
    taps_all = taps_all.reshape(copies, ch, -1, piece)
    taps_full = jnp.transpose(taps_all, (1, 2, 0, 3)).reshape(ch, -1)
    n = taps_full.shape[1]
    tables = dft_tables(n // SIDE)
    spec_h = spectrum(taps_full, tables)
    spec_g = spectrum(gated_spread, tables)
    conv = inverse_prefix(spec_g, spec_h, tables, n)
    back = lax.all_to_all(conv, "seq", split_axis=1, concat_axis=0, tiled=True)
    total = back.T + skip_gain[None, :] * gated
    return (out_gate.astype(jnp.float32) * total).astype(jnp.bfloat16)


def solution(mesh):
    in_specs = (
        P(("grp", "seq"), None),
        P(("grp", "seq"), None),
        P(("grp", "seq"), None),
        P("seq", None),
        P(),
    )
    out_specs = P(("grp", "seq"), None)
    return jax.shard_map(local, mesh=mesh, in_specs=in_specs, out_specs=out_specs, check_vma=False)
```

```python
import jax
import jax.numpy as jnp
from jax import lax
from jax.sharding import PartitionSpec as P

exact_mode = lax.Precision.HIGH


def angle_table(rows, cols, period):
    product = jnp.arange(rows, dtype=jnp.int32)[:, None] * jnp.arange(cols, dtype=jnp.int32)[None, :]
    return (product % period).astype(jnp.float32) * (2.0 * jnp.pi / period)


def dft_tables(side, filled):
    first = angle_table(side, filled, side)
    stage_a = jnp.concatenate([jnp.cos(first), -jnp.sin(first)], axis=0)
    second = angle_table(side, side, side)
    cos_b, sin_b = jnp.cos(second), jnp.sin(second)
    forward_b = jnp.block([[cos_b, -sin_b], [sin_b, cos_b]])
    inverse_b = jnp.block([[cos_b, sin_b], [-sin_b, cos_b]])
    twist = angle_table(side, side, side * side)
    return stage_a, forward_b, inverse_b, jnp.cos(twist), jnp.sin(twist)


def causal_conv(signals, taps_count):
    _, ch, n = signals.shape
    side = 128
    filled = n // side
    stage_a, forward_b, inverse_b, twist_cos, twist_sin = dft_tables(side, filled)
    x = signals.reshape(2 * ch, filled, side)
    a = jnp.einsum("kn,bnm->bkm", stage_a, x, precision=exact_mode)
    a_re, a_im = a[:, :side], a[:, side:]
    b_re = a_re * twist_cos + a_im * twist_sin
    b_im = a_im * twist_cos - a_re * twist_sin
    spec = jnp.einsum(
        "bkm,mj->bkj", jnp.concatenate([b_re, b_im], axis=-1), forward_b, precision=exact_mode
    )
    g_re, g_im = spec[:ch, :, :side], spec[:ch, :, side:]
    h_re, h_im = spec[ch:, :, :side], spec[ch:, :, side:]
    prod = jnp.concatenate([g_re * h_re - g_im * h_im, g_re * h_im + g_im * h_re], axis=-1)
    q = jnp.einsum("bkj,jm->bkm", prod, inverse_b, precision=exact_mode)
    q_re, q_im = q[..., :side], q[..., side:]
    r_re = q_re * twist_cos - q_im * twist_sin
    r_im = q_im * twist_cos + q_re * twist_sin
    y = jnp.einsum(
        "kn,bkm->bnm", stage_a, jnp.concatenate([r_re, r_im], axis=1), precision=exact_mode
    )
    return y.reshape(ch, n) * (1.0 / (side * side))


def local(in_gate, values, out_gate, filter_taps, skip_gain):
    gated = in_gate.astype(jnp.float32) * values.astype(jnp.float32)
    taps = filter_taps.astype(jnp.float32)
    both = jnp.stack([gated.T, taps.T])
    spread = lax.all_to_all(both, "seq", split_axis=1, concat_axis=2, tiled=True)
    conv = causal_conv(spread, spread.shape[2])
    back = lax.all_to_all(conv, "seq", split_axis=1, concat_axis=0, tiled=True)
    total = back.T + skip_gain[None, :] * gated
    return (out_gate.astype(jnp.float32) * total).astype(jnp.bfloat16)


def solution(mesh):
    in_specs = (
        P(("grp", "seq"), None),
        P(("grp", "seq"), None),
        P(("grp", "seq"), None),
        P("seq", None),
        P(),
    )
    out_specs = P(("grp", "seq"), None)
    return jax.shard_map(local, mesh=mesh, in_specs=in_specs, out_specs=out_specs, check_vma=False)
```

```python
import jax
import jax.numpy as jnp
from jax import lax
from jax.sharding import PartitionSpec as P

exact_mode = lax.Precision.HIGH
SIDE = 128


def angle_table(rows, cols, period):
    product = jnp.arange(rows, dtype=jnp.int32)[:, None] * jnp.arange(cols, dtype=jnp.int32)[None, :]
    return (product % period).astype(jnp.float32) * (2.0 * jnp.pi / period)


def dft_tables(filled):
    first = angle_table(SIDE, filled, SIDE)
    stage_a = jnp.concatenate([jnp.cos(first), -jnp.sin(first)], axis=0)
    second = angle_table(SIDE, SIDE, SIDE)
    cos_b, sin_b = jnp.cos(second), jnp.sin(second)
    forward_b = jnp.block([[cos_b, -sin_b], [sin_b, cos_b]])
    inverse_b = jnp.block([[cos_b, sin_b], [-sin_b, cos_b]])
    twist = angle_table(SIDE, SIDE, SIDE * SIDE)
    return stage_a, forward_b, inverse_b, jnp.cos(twist), jnp.sin(twist)


def spectrum(signal, tables):
    stage_a, forward_b, _, twist_cos, twist_sin = tables
    ch, n = signal.shape
    x = signal.reshape(ch, n // SIDE, SIDE)
    a = jnp.einsum("kn,bnm->bkm", stage_a, x, precision=exact_mode)
    a_re, a_im = a[:, :SIDE], a[:, SIDE:]
    b_re = a_re * twist_cos + a_im * twist_sin
    b_im = a_im * twist_cos - a_re * twist_sin
    return jnp.einsum(
        "bkm,mj->bkj", jnp.concatenate([b_re, b_im], axis=-1), forward_b, precision=exact_mode
    )


def inverse_prefix(spec_g, spec_h, tables, n):
    stage_a, _, inverse_b, twist_cos, twist_sin = tables
    ch = spec_g.shape[0]
    g_re, g_im = spec_g[..., :SIDE], spec_g[..., SIDE:]
    h_re, h_im = spec_h[..., :SIDE], spec_h[..., SIDE:]
    prod = jnp.concatenate([g_re * h_re - g_im * h_im, g_re * h_im + g_im * h_re], axis=-1)
    q = jnp.einsum("bkj,jm->bkm", prod, inverse_b, precision=exact_mode)
    q_re, q_im = q[..., :SIDE], q[..., SIDE:]
    r_re = q_re * twist_cos - q_im * twist_sin
    r_im = q_im * twist_cos + q_re * twist_sin
    y = jnp.einsum(
        "kn,bkm->bnm", stage_a, jnp.concatenate([r_re, r_im], axis=1), precision=exact_mode
    )
    return y.reshape(ch, n) * (1.0 / (SIDE * SIDE))


def local(in_gate, values, out_gate, filter_taps, skip_gain):
    own_rows, channels = in_gate.shape
    copies = lax.axis_size("grp")
    core = lax.axis_index("grp") % 2
    half = own_rows // 2
    gated = in_gate.astype(jnp.float32) * values.astype(jnp.float32)
    taps_half = lax.dynamic_slice_in_dim(filter_taps, core * half, half, axis=0)
    payload = jnp.concatenate([gated.T, taps_half.astype(jnp.float32).T], axis=1)
    spread = lax.all_to_all(payload, "seq", split_axis=0, concat_axis=1, tiled=True)
    ch = spread.shape[0]
    spread = spread.reshape(ch, -1, own_rows + half)
    gated_spread = spread[:, :, :own_rows].reshape(ch, -1)
    mine = spread[:, :, own_rows:]
    theirs = lax.ppermute(mine, "grp", [(g, g ^ 1) for g in range(copies)])
    n = gated_spread.shape[1]
    tables = dft_tables(n // SIDE)
    spec_g = spectrum(gated_spread, tables)
    first = jnp.where(core == 0, mine, theirs)
    second = jnp.where(core == 0, theirs, mine)
    taps_full = jnp.stack([first, second], axis=2).reshape(ch, -1)
    spec_h = spectrum(taps_full, tables)
    conv = inverse_prefix(spec_g, spec_h, tables, n)
    back = lax.all_to_all(conv, "seq", split_axis=1, concat_axis=0, tiled=True)
    total = back.T + skip_gain[None, :] * gated
    return (out_gate.astype(jnp.float32) * total).astype(jnp.bfloat16)


def solution(mesh):
    in_specs = (
        P(("grp", "seq"), None),
        P(("grp", "seq"), None),
        P(("grp", "seq"), None),
        P("seq", None),
        P(),
    )
    out_specs = P(("grp", "seq"), None)
    return jax.shard_map(local, mesh=mesh, in_specs=in_specs, out_specs=out_specs, check_vma=False)
```

```python
import jax
import jax.numpy as jnp
from jax import lax
from jax.sharding import PartitionSpec as P

exact_mode = lax.Precision.HIGH
SIDE = 128


def angle_table(rows, cols, period):
    product = jnp.arange(rows, dtype=jnp.int32)[:, None] * jnp.arange(cols, dtype=jnp.int32)[None, :]
    return (product % period).astype(jnp.float32) * (2.0 * jnp.pi / period)


def dft_tables(filled):
    first = angle_table(SIDE, filled, SIDE)
    stage_a = jnp.concatenate([jnp.cos(first), -jnp.sin(first)], axis=0)
    second = angle_table(SIDE, SIDE, SIDE)
    cos_b, sin_b = jnp.cos(second), jnp.sin(second)
    forward_b = jnp.block([[cos_b, -sin_b], [sin_b, cos_b]])
    inverse_b = jnp.block([[cos_b, sin_b], [-sin_b, cos_b]])
    twist = angle_table(SIDE, SIDE, SIDE * SIDE)
    return stage_a, forward_b, inverse_b, jnp.cos(twist), jnp.sin(twist)


def spectrum(signal, tables):
    stage_a, forward_b, _, twist_cos, twist_sin = tables
    ch, n = signal.shape
    x = signal.reshape(ch, n // SIDE, SIDE)
    a = jnp.einsum("kn,bnm->bkm", stage_a, x, precision=exact_mode)
    a_re, a_im = a[:, :SIDE], a[:, SIDE:]
    b_re = a_re * twist_cos + a_im * twist_sin
    b_im = a_im * twist_cos - a_re * twist_sin
    return jnp.einsum(
        "bkm,mj->bkj", jnp.concatenate([b_re, b_im], axis=-1), forward_b, precision=exact_mode
    )


def inverse_prefix(spec_g, spec_h, tables, n):
    stage_a, _, inverse_b, twist_cos, twist_sin = tables
    ch = spec_g.shape[0]
    g_re, g_im = spec_g[..., :SIDE], spec_g[..., SIDE:]
    h_re, h_im = spec_h[..., :SIDE], spec_h[..., SIDE:]
    prod = jnp.concatenate([g_re * h_re - g_im * h_im, g_re * h_im + g_im * h_re], axis=-1)
    q = jnp.einsum("bkj,jm->bkm", prod, inverse_b, precision=exact_mode)
    q_re, q_im = q[..., :SIDE], q[..., SIDE:]
    r_re = q_re * twist_cos - q_im * twist_sin
    r_im = q_im * twist_cos + q_re * twist_sin
    y = jnp.einsum(
        "kn,bkm->bnm", stage_a, jnp.concatenate([r_re, r_im], axis=1), precision=exact_mode
    )
    return y.reshape(ch, n) * (1.0 / (SIDE * SIDE))


def local(in_gate, values, out_gate, filter_taps, skip_gain):
    own_rows, channels = in_gate.shape
    copies = lax.axis_size("grp")
    copy_index = lax.axis_index("grp")
    groups = lax.axis_size("seq")
    ch = channels // groups
    share = ch // copies
    gated = in_gate.astype(jnp.float32) * values.astype(jnp.float32)
    taps = filter_taps.astype(jnp.float32).reshape(own_rows, groups, copies, share)
    taps_part = lax.dynamic_index_in_dim(taps, copy_index, axis=2, keepdims=False)
    payload = jnp.concatenate(
        [gated.T.reshape(groups, ch, own_rows), jnp.transpose(taps_part, (1, 2, 0))], axis=1
    )
    spread = lax.all_to_all(payload, "seq", split_axis=0, concat_axis=0, tiled=True)
    gated_spread = jnp.transpose(spread[:, :ch], (1, 0, 2)).reshape(ch, -1)
    mine = jnp.transpose(spread[:, ch:], (1, 0, 2)).reshape(share, -1)
    arrived = [mine] + [
        lax.ppermute(mine, "grp", [(g, (g + d) % copies) for g in range(copies)])
        for d in range(1, copies)
    ]
    n = gated_spread.shape[1]
    tables = dft_tables(n // SIDE)
    spec_g = spectrum(gated_spread, tables)
    order = (copy_index - jnp.arange(copies, dtype=jnp.int32)) % copies
    taps_full = jnp.take(jnp.stack(arrived), order, axis=0).reshape(ch, n)
    spec_h = spectrum(taps_full, tables)
    conv = inverse_prefix(spec_g, spec_h, tables, n)
    back = lax.all_to_all(conv, "seq", split_axis=1, concat_axis=0, tiled=True)
    total = back.T + skip_gain[None, :] * gated
    return (out_gate.astype(jnp.float32) * total).astype(jnp.bfloat16)


def solution(mesh):
    in_specs = (
        P(("grp", "seq"), None),
        P(("grp", "seq"), None),
        P(("grp", "seq"), None),
        P("seq", None),
        P(),
    )
    out_specs = P(("grp", "seq"), None)
    return jax.shard_map(local, mesh=mesh, in_specs=in_specs, out_specs=out_specs, check_vma=False)
```

```python
import jax
import jax.numpy as jnp
from jax import lax
from jax.experimental import pallas as pl
from jax.experimental.pallas import tpu as pltpu
from jax.sharding import PartitionSpec as P

exact_mode = lax.Precision.HIGH
SIDE = 128


def angle_table(rows, cols, period):
    product = jnp.arange(rows, dtype=jnp.int32)[:, None] * jnp.arange(cols, dtype=jnp.int32)[None, :]
    return (product % period).astype(jnp.float32) * (2.0 * jnp.pi / period)


def dft_tables(filled):
    first = angle_table(SIDE, filled, SIDE)
    stage_a = jnp.concatenate([jnp.cos(first), -jnp.sin(first)], axis=0)
    second = angle_table(SIDE, SIDE, SIDE)
    cos_b, sin_b = jnp.cos(second), jnp.sin(second)
    forward_b = jnp.block([[cos_b, -sin_b], [sin_b, cos_b]])
    inverse_b = jnp.block([[cos_b, sin_b], [-sin_b, cos_b]])
    twist = angle_table(SIDE, SIDE, SIDE * SIDE)
    return stage_a, forward_b, inverse_b, jnp.cos(twist), jnp.sin(twist)


def spectrum(signal, tables):
    stage_a, forward_b, _, twist_cos, twist_sin = tables
    ch, n = signal.shape
    x = signal.reshape(ch, n // SIDE, SIDE)
    a = jnp.einsum("kn,bnm->bkm", stage_a, x, precision=exact_mode)
    a_re, a_im = a[:, :SIDE], a[:, SIDE:]
    b_re = a_re * twist_cos + a_im * twist_sin
    b_im = a_im * twist_cos - a_re * twist_sin
    return jnp.einsum(
        "bkm,mj->bkj", jnp.concatenate([b_re, b_im], axis=-1), forward_b, precision=exact_mode
    )


def inverse_prefix(spec_g, spec_h, tables, n):
    stage_a, _, inverse_b, twist_cos, twist_sin = tables
    ch = spec_g.shape[0]
    g_re, g_im = spec_g[..., :SIDE], spec_g[..., SIDE:]
    h_re, h_im = spec_h[..., :SIDE], spec_h[..., SIDE:]
    prod = jnp.concatenate([g_re * h_re - g_im * h_im, g_re * h_im + g_im * h_re], axis=-1)
    q = jnp.einsum("bkj,jm->bkm", prod, inverse_b, precision=exact_mode)
    q_re, q_im = q[..., :SIDE], q[..., SIDE:]
    r_re = q_re * twist_cos - q_im * twist_sin
    r_im = q_im * twist_cos + q_re * twist_sin
    y = jnp.einsum(
        "kn,bkm->bnm", stage_a, jnp.concatenate([r_re, r_im], axis=1), precision=exact_mode
    )
    return y.reshape(ch, n) * (1.0 / (SIDE * SIDE))


def prologue_kernel(gate_ref, values_ref, taps_ref, out_ref):
    rows = gate_ref.shape[0]
    gated = gate_ref[...].astype(jnp.float32) * values_ref[...].astype(jnp.float32)
    out_ref[:, :rows] = gated.T
    out_ref[:, rows:] = taps_ref[...].astype(jnp.float32).T


def epilogue_kernel(back_ref, gate_ref, values_ref, out_gate_ref, skip_ref, out_ref):
    gated = gate_ref[...].astype(jnp.float32) * values_ref[...].astype(jnp.float32)
    total = back_ref[...].T + skip_ref[...] * gated
    out_ref[...] = (out_gate_ref[...].astype(jnp.float32) * total).astype(out_ref.dtype)


def vmem_call(kernel, out_shape, count):
    return pl.pallas_call(
        kernel,
        out_shape=out_shape,
        in_specs=[pl.BlockSpec(memory_space=pltpu.VMEM)] * count,
        out_specs=pl.BlockSpec(memory_space=pltpu.VMEM),
    )


def local(in_gate, values, out_gate, filter_taps, skip_gain):
    own_rows, channels = in_gate.shape
    copies = lax.axis_size("grp")
    core = lax.axis_index("grp") % 2
    half = own_rows // 2
    taps_half = lax.dynamic_slice_in_dim(filter_taps, core * half, half, axis=0)
    payload = vmem_call(
        prologue_kernel, jax.ShapeDtypeStruct((channels, own_rows + half), jnp.float32), 3
    )(in_gate, values, taps_half)
    spread = lax.all_to_all(payload, "seq", split_axis=0, concat_axis=1, tiled=True)
    ch = spread.shape[0]
    spread = spread.reshape(ch, -1, own_rows + half)
    gated_spread = spread[:, :, :own_rows].reshape(ch, -1)
    mine = spread[:, :, own_rows:]
    theirs = lax.ppermute(mine, "grp", [(g, g ^ 1) for g in range(copies)])
    n = gated_spread.shape[1]
    tables = dft_tables(n // SIDE)
    spec_g = spectrum(gated_spread, tables)
    first = jnp.where(core == 0, mine, theirs)
    second = jnp.where(core == 0, theirs, mine)
    taps_full = jnp.stack([first, second], axis=2).reshape(ch, -1)
    spec_h = spectrum(taps_full, tables)
    conv = inverse_prefix(spec_g, spec_h, tables, n)
    back = lax.all_to_all(conv, "seq", split_axis=1, concat_axis=0, tiled=True)
    return vmem_call(epilogue_kernel, jax.ShapeDtypeStruct(in_gate.shape, jnp.bfloat16), 5)(
        back, in_gate, values, out_gate, skip_gain.reshape(1, channels)
    )


def solution(mesh):
    in_specs = (
        P(("grp", "seq"), None),
        P(("grp", "seq"), None),
        P(("grp", "seq"), None),
        P("seq", None),
        P(),
    )
    out_specs = P(("grp", "seq"), None)
    return jax.shard_map(local, mesh=mesh, in_specs=in_specs, out_specs=out_specs, check_vma=False)
```

```python
import jax
import jax.numpy as jnp
from jax import lax
from jax.experimental import pallas as pl
from jax.experimental.pallas import tpu as pltpu
from jax.sharding import PartitionSpec as P

exact_mode = lax.Precision.HIGH
SIDE = 128


def angle_table(rows, cols, period):
    product = jnp.arange(rows, dtype=jnp.int32)[:, None] * jnp.arange(cols, dtype=jnp.int32)[None, :]
    return (product % period).astype(jnp.float32) * (2.0 * jnp.pi / period)


def dft_tables(filled):
    first = angle_table(SIDE, filled, SIDE)
    stage_a = jnp.concatenate([jnp.cos(first), -jnp.sin(first)], axis=0)
    second = angle_table(SIDE, SIDE, SIDE)
    cos_b, sin_b = jnp.cos(second), jnp.sin(second)
    forward_b = jnp.block([[cos_b, -sin_b], [sin_b, cos_b]])
    inverse_b = jnp.block([[cos_b, sin_b], [-sin_b, cos_b]])
    twist = angle_table(SIDE, SIDE, SIDE * SIDE)
    return stage_a, forward_b, inverse_b, jnp.cos(twist), jnp.sin(twist)


def spectrum(signal, tables):
    stage_a, forward_b, _, twist_cos, twist_sin = tables
    ch, n = signal.shape
    x = signal.reshape(ch, n // SIDE, SIDE)
    a = jnp.einsum("kn,bnm->bkm", stage_a, x, precision=exact_mode)
    a_re, a_im = a[:, :SIDE], a[:, SIDE:]
    b_re = a_re * twist_cos + a_im * twist_sin
    b_im = a_im * twist_cos - a_re * twist_sin
    return jnp.einsum(
        "bkm,mj->bkj", jnp.concatenate([b_re, b_im], axis=-1), forward_b, precision=exact_mode
    )


def inverse_prefix(spec_g, spec_h, tables, n):
    stage_a, _, inverse_b, twist_cos, twist_sin = tables
    ch = spec_g.shape[0]
    g_re, g_im = spec_g[..., :SIDE], spec_g[..., SIDE:]
    h_re, h_im = spec_h[..., :SIDE], spec_h[..., SIDE:]
    prod = jnp.concatenate([g_re * h_re - g_im * h_im, g_re * h_im + g_im * h_re], axis=-1)
    q = jnp.einsum("bkj,jm->bkm", prod, inverse_b, precision=exact_mode)
    q_re, q_im = q[..., :SIDE], q[..., SIDE:]
    r_re = q_re * twist_cos - q_im * twist_sin
    r_im = q_im * twist_cos + q_re * twist_sin
    y = jnp.einsum(
        "kn,bkm->bnm", stage_a, jnp.concatenate([r_re, r_im], axis=1), precision=exact_mode
    )
    return y.reshape(ch, n) * (1.0 / (SIDE * SIDE))


def prologue_kernel(core_ref, gate_ref, values_ref, taps_ref, out_ref):
    step = pl.program_id(0)
    gated_steps = pl.num_programs(0) - 1

    @pl.when(step < gated_steps)
    def _():
        gated = gate_ref[...].astype(jnp.float32) * values_ref[...].astype(jnp.float32)
        out_ref[...] = gated.T

    @pl.when(step == gated_steps)
    def _():
        out_ref[...] = taps_ref[...].astype(jnp.float32).T


def epilogue_kernel(back_ref, gate_ref, values_ref, out_gate_ref, skip_ref, out_ref):
    gated = gate_ref[...].astype(jnp.float32) * values_ref[...].astype(jnp.float32)
    total = back_ref[...].T + skip_ref[...] * gated
    out_ref[...] = (out_gate_ref[...].astype(jnp.float32) * total).astype(out_ref.dtype)


def prologue(core, in_gate, values, filter_taps):
    rows, channels = in_gate.shape
    half = rows // 2
    gated_steps = rows // half
    last = gated_steps - 1
    row_block = pl.BlockSpec((half, channels), lambda j, c: (jnp.minimum(j, last), 0))
    taps_block = pl.BlockSpec((half, channels), lambda j, c: (c[0], 0))
    grid_spec = pltpu.PrefetchScalarGridSpec(
        num_scalar_prefetch=1,
        grid=(gated_steps + 1,),
        in_specs=[row_block, row_block, taps_block],
        out_specs=pl.BlockSpec((channels, half), lambda j, c: (0, j)),
    )
    return pl.pallas_call(
        prologue_kernel,
        grid_spec=grid_spec,
        out_shape=jax.ShapeDtypeStruct((channels, rows + half), jnp.float32),
    )(core.reshape(1), in_gate, values, filter_taps)


def epilogue(back, in_gate, values, out_gate, skip_gain):
    rows, channels = in_gate.shape
    width = 128
    col_block = pl.BlockSpec((rows, width), lambda j: (0, j))
    return pl.pallas_call(
        epilogue_kernel,
        grid=(channels // width,),
        in_specs=[
            pl.BlockSpec((width, rows), lambda j: (j, 0)),
            col_block,
            col_block,
            col_block,
            pl.BlockSpec((1, width), lambda j: (0, j)),
        ],
        out_specs=col_block,
        out_shape=jax.ShapeDtypeStruct((rows, channels), jnp.bfloat16),
    )(back, in_gate, values, out_gate, skip_gain.reshape(1, channels))


def local(in_gate, values, out_gate, filter_taps, skip_gain):
    own_rows, channels = in_gate.shape
    copies = lax.axis_size("grp")
    core = lax.axis_index("grp") % 2
    half = own_rows // 2
    payload = prologue(core.astype(jnp.int32), in_gate, values, filter_taps)
    spread = lax.all_to_all(payload, "seq", split_axis=0, concat_axis=1, tiled=True)
    ch = spread.shape[0]
    spread = spread.reshape(ch, -1, own_rows + half)
    gated_spread = spread[:, :, :own_rows].reshape(ch, -1)
    mine = spread[:, :, own_rows:]
    theirs = lax.ppermute(mine, "grp", [(g, g ^ 1) for g in range(copies)])
    n = gated_spread.shape[1]
    tables = dft_tables(n // SIDE)
    spec_g = spectrum(gated_spread, tables)
    first = jnp.where(core == 0, mine, theirs)
    second = jnp.where(core == 0, theirs, mine)
    taps_full = jnp.stack([first, second], axis=2).reshape(ch, -1)
    spec_h = spectrum(taps_full, tables)
    conv = inverse_prefix(spec_g, spec_h, tables, n)
    back = lax.all_to_all(conv, "seq", split_axis=1, concat_axis=0, tiled=True)
    return epilogue(back, in_gate, values, out_gate, skip_gain)


def solution(mesh):
    in_specs = (
        P(("grp", "seq"), None),
        P(("grp", "seq"), None),
        P(("grp", "seq"), None),
        P("seq", None),
        P(),
    )
    out_specs = P(("grp", "seq"), None)
    return jax.shard_map(local, mesh=mesh, in_specs=in_specs, out_specs=out_specs, check_vma=False)
```

```python
import jax
import jax.numpy as jnp
from jax import lax
from jax.experimental import pallas as pl
from jax.experimental.pallas import tpu as pltpu
from jax.sharding import PartitionSpec as P

exact_mode = lax.Precision.HIGH
SIDE = 128


def angle_table(rows, cols, period):
    product = jnp.arange(rows, dtype=jnp.int32)[:, None] * jnp.arange(cols, dtype=jnp.int32)[None, :]
    return (product % period).astype(jnp.float32) * (2.0 * jnp.pi / period)


def dft_tables(filled):
    first = angle_table(SIDE, filled, SIDE)
    stage_a = jnp.concatenate([jnp.cos(first), -jnp.sin(first)], axis=0)
    second = angle_table(SIDE, SIDE, SIDE)
    cos_b, sin_b = jnp.cos(second), jnp.sin(second)
    forward_b = jnp.block([[cos_b, -sin_b], [sin_b, cos_b]])
    inverse_b = jnp.block([[cos_b, sin_b], [-sin_b, cos_b]])
    twist = angle_table(SIDE, SIDE, SIDE * SIDE)
    return stage_a, forward_b, inverse_b, jnp.cos(twist), jnp.sin(twist)


def spectrum(signal, tables):
    stage_a, forward_b, _, twist_cos, twist_sin = tables
    ch, n = signal.shape
    x = signal.reshape(ch, n // SIDE, SIDE)
    a = jnp.einsum("kn,bnm->bkm", stage_a, x, precision=exact_mode)
    a_re, a_im = a[:, :SIDE], a[:, SIDE:]
    b_re = a_re * twist_cos + a_im * twist_sin
    b_im = a_im * twist_cos - a_re * twist_sin
    return jnp.einsum(
        "bkm,mj->bkj", jnp.concatenate([b_re, b_im], axis=-1), forward_b, precision=exact_mode
    )


def inverse_prefix(spec_g, spec_h, tables, n):
    stage_a, _, inverse_b, twist_cos, twist_sin = tables
    ch = spec_g.shape[0]
    g_re, g_im = spec_g[..., :SIDE], spec_g[..., SIDE:]
    h_re, h_im = spec_h[..., :SIDE], spec_h[..., SIDE:]
    prod = jnp.concatenate([g_re * h_re - g_im * h_im, g_re * h_im + g_im * h_re], axis=-1)
    q = jnp.einsum("bkj,jm->bkm", prod, inverse_b, precision=exact_mode)
    q_re, q_im = q[..., :SIDE], q[..., SIDE:]
    r_re = q_re * twist_cos - q_im * twist_sin
    r_im = q_im * twist_cos + q_re * twist_sin
    y = jnp.einsum(
        "kn,bkm->bnm", stage_a, jnp.concatenate([r_re, r_im], axis=1), precision=exact_mode
    )
    return y.reshape(ch, n) * (1.0 / (SIDE * SIDE))


def prologue_kernel(core_ref, gate_ref, values_ref, taps_ref, out_ref):
    step = pl.program_id(0)
    gated_steps = pl.num_programs(0) - 1

    @pl.when(step < gated_steps)
    def _():
        gated = gate_ref[...].astype(jnp.float32) * values_ref[...].astype(jnp.float32)
        out_ref[...] = gated.T

    @pl.when(step == gated_steps)
    def _():
        out_ref[...] = taps_ref[...].astype(jnp.float32).T


def prologue(core, in_gate, values, filter_taps):
    rows, channels = in_gate.shape
    half = rows // 2
    gated_steps = rows // half
    last = gated_steps - 1
    row_block = pl.BlockSpec((half, channels), lambda j, c: (jnp.minimum(j, last), 0))
    taps_block = pl.BlockSpec((half, channels), lambda j, c: (c[0], 0))
    grid_spec = pltpu.PrefetchScalarGridSpec(
        num_scalar_prefetch=1,
        grid=(gated_steps + 1,),
        in_specs=[row_block, row_block, taps_block],
        out_specs=pl.BlockSpec((channels, half), lambda j, c: (0, j)),
    )
    return pl.pallas_call(
        prologue_kernel,
        grid_spec=grid_spec,
        out_shape=jax.ShapeDtypeStruct((channels, rows + half), jnp.float32),
    )(core.reshape(1), in_gate, values, filter_taps)


def local(in_gate, values, out_gate, filter_taps, skip_gain):
    own_rows, channels = in_gate.shape
    copies = lax.axis_size("grp")
    core = lax.axis_index("grp") % 2
    half = own_rows // 2
    payload = prologue(core.astype(jnp.int32), in_gate, values, filter_taps)
    spread = lax.all_to_all(payload, "seq", split_axis=0, concat_axis=1, tiled=True)
    ch = spread.shape[0]
    spread = spread.reshape(ch, -1, own_rows + half)
    gated_spread = spread[:, :, :own_rows].reshape(ch, -1)
    mine = spread[:, :, own_rows:]
    theirs = lax.ppermute(mine, "grp", [(g, g ^ 1) for g in range(copies)])
    n = gated_spread.shape[1]
    tables = dft_tables(n // SIDE)
    spec_g = spectrum(gated_spread, tables)
    first = jnp.where(core == 0, mine, theirs)
    second = jnp.where(core == 0, theirs, mine)
    taps_full = jnp.stack([first, second], axis=2).reshape(ch, -1)
    spec_h = spectrum(taps_full, tables)
    conv = inverse_prefix(spec_g, spec_h, tables, n)
    back = lax.all_to_all(conv, "seq", split_axis=1, concat_axis=0, tiled=True)
    gated = in_gate.astype(jnp.float32) * values.astype(jnp.float32)
    total = back.T + skip_gain[None, :] * gated
    return (out_gate.astype(jnp.float32) * total).astype(jnp.bfloat16)


def solution(mesh):
    in_specs = (
        P(("grp", "seq"), None),
        P(("grp", "seq"), None),
        P(("grp", "seq"), None),
        P("seq", None),
        P(),
    )
    out_specs = P(("grp", "seq"), None)
    return jax.shard_map(local, mesh=mesh, in_specs=in_specs, out_specs=out_specs, check_vma=False)
```

```python
import jax
import jax.numpy as jnp
from jax import lax
from jax.experimental import pallas as pl
from jax.experimental.pallas import tpu as pltpu
from jax.sharding import PartitionSpec as P

exact_mode = lax.Precision.HIGH
SIDE = 128


def angle_table(rows, cols, period):
    product = jnp.arange(rows, dtype=jnp.int32)[:, None] * jnp.arange(cols, dtype=jnp.int32)[None, :]
    return (product % period).astype(jnp.float32) * (2.0 * jnp.pi / period)


def dft_tables(filled):
    rows = SIDE // 2 + 8
    first = angle_table(rows, filled, SIDE)
    stage_a = jnp.concatenate([jnp.cos(first), -jnp.sin(first)], axis=0)
    second = angle_table(SIDE, SIDE, SIDE)
    cos_b, sin_b = jnp.cos(second), jnp.sin(second)
    forward_b = jnp.block([[cos_b, -sin_b], [sin_b, cos_b]])
    inverse_b = jnp.block([[cos_b, sin_b], [-sin_b, cos_b]])
    twist = angle_table(rows, SIDE, SIDE * SIDE)
    row = jnp.arange(rows, dtype=jnp.int32)
    weight = jnp.where((row == 0) | (row == SIDE // 2), 1.0, jnp.where(row < SIDE // 2, 2.0, 0.0))
    stage_inv = stage_a * jnp.concatenate([weight, weight])[:, None]
    return stage_a, forward_b, inverse_b, jnp.cos(twist), jnp.sin(twist), stage_inv


def spectrum(signal, tables):
    stage_a, forward_b, _, twist_cos, twist_sin, _ = tables
    rows = twist_cos.shape[0]
    ch, n = signal.shape
    x = signal.reshape(ch, n // SIDE, SIDE)
    a = jnp.einsum("kn,bnm->bkm", stage_a, x, precision=exact_mode)
    a_re, a_im = a[:, :rows], a[:, rows:]
    b_re = a_re * twist_cos + a_im * twist_sin
    b_im = a_im * twist_cos - a_re * twist_sin
    return jnp.einsum(
        "bkm,mj->bkj", jnp.concatenate([b_re, b_im], axis=-1), forward_b, precision=exact_mode
    )


def inverse_prefix(spec_g, spec_h, tables, n):
    _, _, inverse_b, twist_cos, twist_sin, stage_inv = tables
    g_re, g_im = spec_g[..., :SIDE], spec_g[..., SIDE:]
    h_re, h_im = spec_h[..., :SIDE], spec_h[..., SIDE:]
    prod = jnp.concatenate([g_re * h_re - g_im * h_im, g_re * h_im + g_im * h_re], axis=-1)
    q = jnp.einsum("bkj,jm->bkm", prod, inverse_b, precision=exact_mode)
    q_re, q_im = q[..., :SIDE], q[..., SIDE:]
    r_re = q_re * twist_cos - q_im * twist_sin
    r_im = q_im * twist_cos + q_re * twist_sin
    y = jnp.einsum(
        "kn,bkm->bnm", stage_inv, jnp.concatenate([r_re, r_im], axis=1), precision=exact_mode
    )
    return y.reshape(y.shape[0], n) * (1.0 / (SIDE * SIDE))


def prologue_kernel(core_ref, gate_ref, values_ref, taps_ref, out_ref):
    step = pl.program_id(0)
    gated_steps = pl.num_programs(0) - 1

    @pl.when(step < gated_steps)
    def _():
        gated = gate_ref[...].astype(jnp.float32) * values_ref[...].astype(jnp.float32)
        out_ref[...] = gated.T

    @pl.when(step == gated_steps)
    def _():
        out_ref[...] = taps_ref[...].astype(jnp.float32).T


def prologue(core, in_gate, values, filter_taps):
    rows, channels = in_gate.shape
    half = rows // 2
    gated_steps = rows // half
    last = gated_steps - 1
    row_block = pl.BlockSpec((half, channels), lambda j, c: (jnp.minimum(j, last), 0))
    taps_block = pl.BlockSpec((half, channels), lambda j, c: (c[0], 0))
    grid_spec = pltpu.PrefetchScalarGridSpec(
        num_scalar_prefetch=1,
        grid=(gated_steps + 1,),
        in_specs=[row_block, row_block, taps_block],
        out_specs=pl.BlockSpec((channels, half), lambda j, c: (0, j)),
    )
    return pl.pallas_call(
        prologue_kernel,
        grid_spec=grid_spec,
        out_shape=jax.ShapeDtypeStruct((channels, rows + half), jnp.float32),
    )(core.reshape(1), in_gate, values, filter_taps)


def local(in_gate, values, out_gate, filter_taps, skip_gain):
    own_rows, channels = in_gate.shape
    copies = lax.axis_size("grp")
    core = lax.axis_index("grp") % 2
    half = own_rows // 2
    payload = prologue(core.astype(jnp.int32), in_gate, values, filter_taps)
    spread = lax.all_to_all(payload, "seq", split_axis=0, concat_axis=1, tiled=True)
    ch = spread.shape[0]
    spread = spread.reshape(ch, -1, own_rows + half)
    gated_spread = spread[:, :, :own_rows].reshape(ch, -1)
    mine = spread[:, :, own_rows:]
    theirs = lax.ppermute(mine, "grp", [(g, g ^ 1) for g in range(copies)])
    n = gated_spread.shape[1]
    tables = dft_tables(n // SIDE)
    spec_g = spectrum(gated_spread, tables)
    first = jnp.where(core == 0, mine, theirs)
    second = jnp.where(core == 0, theirs, mine)
    taps_full = jnp.stack([first, second], axis=2).reshape(ch, -1)
    spec_h = spectrum(taps_full, tables)
    conv = inverse_prefix(spec_g, spec_h, tables, n)
    back = lax.all_to_all(conv, "seq", split_axis=1, concat_axis=0, tiled=True)
    gated = in_gate.astype(jnp.float32) * values.astype(jnp.float32)
    total = back.T + skip_gain[None, :] * gated
    return (out_gate.astype(jnp.float32) * total).astype(jnp.bfloat16)


def solution(mesh):
    in_specs = (
        P(("grp", "seq"), None),
        P(("grp", "seq"), None),
        P(("grp", "seq"), None),
        P("seq", None),
        P(),
    )
    out_specs = P(("grp", "seq"), None)
    return jax.shard_map(local, mesh=mesh, in_specs=in_specs, out_specs=out_specs, check_vma=False)
```

```python
import jax
import jax.numpy as jnp
from jax import lax
from jax.experimental import pallas as pl
from jax.experimental.pallas import tpu as pltpu
from jax.sharding import PartitionSpec as P

exact_mode = lax.Precision.HIGH
SIDE = 128


def angle_table(rows, cols, period):
    product = jnp.arange(rows, dtype=jnp.int32)[:, None] * jnp.arange(cols, dtype=jnp.int32)[None, :]
    return (product % period).astype(jnp.float32) * (2.0 * jnp.pi / period)


def dft_tables(filled):
    rows = SIDE // 2 + 8
    first = angle_table(rows, filled, SIDE)
    stage_a = jnp.concatenate([jnp.cos(first), -jnp.sin(first)], axis=0)
    second = angle_table(SIDE, SIDE, SIDE)
    cos_b, sin_b = jnp.cos(second), jnp.sin(second)
    forward_b = jnp.block([[cos_b, -sin_b], [sin_b, cos_b]])
    inverse_b = jnp.block([[cos_b, sin_b], [-sin_b, cos_b]])
    twist = angle_table(rows, SIDE, SIDE * SIDE)
    row = jnp.arange(rows, dtype=jnp.int32)
    weight = jnp.where((row == 0) | (row == SIDE // 2), 1.0, jnp.where(row < SIDE // 2, 2.0, 0.0))
    stage_inv = stage_a * jnp.concatenate([weight, weight])[:, None]
    return stage_a, forward_b, inverse_b, jnp.cos(twist), jnp.sin(twist), stage_inv


def spectrum(signal, tables):
    stage_a, forward_b, _, twist_cos, twist_sin, _ = tables
    rows = twist_cos.shape[0]
    ch, n = signal.shape
    x = signal.reshape(ch, n // SIDE, SIDE)
    a = jnp.einsum("kn,bnm->bkm", stage_a, x, precision=exact_mode)
    a_re, a_im = a[:, :rows], a[:, rows:]
    b_re = a_re * twist_cos + a_im * twist_sin
    b_im = a_im * twist_cos - a_re * twist_sin
    return jnp.einsum(
        "bkm,mj->bkj", jnp.concatenate([b_re, b_im], axis=-1), forward_b, precision=exact_mode
    )


def inverse_prefix(spec_g, spec_h, tables, n):
    _, _, inverse_b, twist_cos, twist_sin, stage_inv = tables
    g_re, g_im = spec_g[..., :SIDE], spec_g[..., SIDE:]
    h_re, h_im = spec_h[..., :SIDE], spec_h[..., SIDE:]
    prod = jnp.concatenate([g_re * h_re - g_im * h_im, g_re * h_im + g_im * h_re], axis=-1)
    q = jnp.einsum("bkj,jm->bkm", prod, inverse_b, precision=exact_mode)
    q_re, q_im = q[..., :SIDE], q[..., SIDE:]
    r_re = q_re * twist_cos - q_im * twist_sin
    r_im = q_im * twist_cos + q_re * twist_sin
    y = jnp.einsum(
        "kn,bkm->bnm", stage_inv, jnp.concatenate([r_re, r_im], axis=1), precision=exact_mode
    )
    return y.reshape(y.shape[0], n) * (1.0 / (SIDE * SIDE))


def split_bf16(x):
    hi = x.astype(jnp.bfloat16)
    return hi, (x - hi.astype(jnp.float32)).astype(jnp.bfloat16)


def dot3_left(w_hi, w_lo, x):
    x_hi, x_lo = split_bf16(x)
    f32 = jnp.float32
    return (
        jnp.dot(w_hi, x_hi, preferred_element_type=f32)
        + jnp.dot(w_lo, x_hi, preferred_element_type=f32)
        + jnp.dot(w_hi, x_lo, preferred_element_type=f32)
    )


def dot3_right(x, w_hi, w_lo):
    x_hi, x_lo = split_bf16(x)
    f32 = jnp.float32
    return (
        jnp.dot(x_hi, w_hi, preferred_element_type=f32)
        + jnp.dot(x_lo, w_hi, preferred_element_type=f32)
        + jnp.dot(x_hi, w_lo, preferred_element_type=f32)
    )


def transform_kernel(
    g_ref, h_ref, a_hi, a_lo, bf_hi, bf_lo, bi_hi, bi_lo, tc_ref, ts_ref, ai_hi, ai_lo, out_ref
):
    rows = tc_ref.shape[0]
    tc, ts = tc_ref[...], ts_ref[...]
    for c in range(g_ref.shape[0]):
        x = jnp.concatenate([g_ref[c], h_ref[c]], axis=1)
        a = dot3_left(a_hi[...], a_lo[...], x)
        parts = []
        for cols in (slice(0, SIDE), slice(SIDE, 2 * SIDE)):
            a_re, a_im = a[:rows, cols], a[rows:, cols]
            b_re = a_re * tc + a_im * ts
            b_im = a_im * tc - a_re * ts
            parts.append(jnp.concatenate([b_re, b_im], axis=1))
        spec = dot3_right(jnp.concatenate(parts, axis=0), bf_hi[...], bf_lo[...])
        g_re, g_im = spec[:rows, :SIDE], spec[:rows, SIDE:]
        h_re, h_im = spec[rows:, :SIDE], spec[rows:, SIDE:]
        prod = jnp.concatenate([g_re * h_re - g_im * h_im, g_re * h_im + g_im * h_re], axis=1)
        q = dot3_right(prod, bi_hi[...], bi_lo[...])
        q_re, q_im = q[:, :SIDE], q[:, SIDE:]
        r = jnp.concatenate([q_re * tc - q_im * ts, q_im * tc + q_re * ts], axis=0)
        out_ref[c] = dot3_left(ai_hi[...], ai_lo[...], r) * (1.0 / (SIDE * SIDE))


def split_table(x):
    hi = lax.reduce_precision(x, exponent_bits=8, mantissa_bits=7)
    return hi.astype(jnp.bfloat16), (x - hi).astype(jnp.bfloat16)


def fused_conv(gated_spread, taps_full):
    ch, n = gated_spread.shape
    filled = n // SIDE
    stage_a, forward_b, inverse_b, twist_cos, twist_sin, stage_inv = dft_tables(filled)
    tables = [
        *split_table(stage_a),
        *split_table(forward_b),
        *split_table(inverse_b),
        twist_cos,
        twist_sin,
        *split_table(stage_inv.T),
    ]
    per_step = 8
    sig_block = pl.BlockSpec((per_step, filled, SIDE), lambda i: (i, 0, 0))
    table_specs = [pl.BlockSpec(t.shape, lambda i: (0, 0)) for t in tables]
    out = pl.pallas_call(
        transform_kernel,
        grid=(ch // per_step,),
        in_specs=[sig_block, sig_block] + table_specs,
        out_specs=sig_block,
        out_shape=jax.ShapeDtypeStruct((ch, filled, SIDE), jnp.float32),
    )(gated_spread.reshape(ch, filled, SIDE), taps_full.reshape(ch, filled, SIDE), *tables)
    return out.reshape(ch, n)


def prologue_kernel(core_ref, gate_ref, values_ref, taps_ref, out_ref):
    step = pl.program_id(0)
    gated_steps = pl.num_programs(0) - 1

    @pl.when(step < gated_steps)
    def _():
        gated = gate_ref[...].astype(jnp.float32) * values_ref[...].astype(jnp.float32)
        out_ref[...] = gated.T

    @pl.when(step == gated_steps)
    def _():
        out_ref[...] = taps_ref[...].astype(jnp.float32).T


def prologue(core, in_gate, values, filter_taps):
    rows, channels = in_gate.shape
    half = rows // 2
    gated_steps = rows // half
    last = gated_steps - 1
    row_block = pl.BlockSpec((half, channels), lambda j, c: (jnp.minimum(j, last), 0))
    taps_block = pl.BlockSpec((half, channels), lambda j, c: (c[0], 0))
    grid_spec = pltpu.PrefetchScalarGridSpec(
        num_scalar_prefetch=1,
        grid=(gated_steps + 1,),
        in_specs=[row_block, row_block, taps_block],
        out_specs=pl.BlockSpec((channels, half), lambda j, c: (0, j)),
    )
    return pl.pallas_call(
        prologue_kernel,
        grid_spec=grid_spec,
        out_shape=jax.ShapeDtypeStruct((channels, rows + half), jnp.float32),
    )(core.reshape(1), in_gate, values, filter_taps)


def local(in_gate, values, out_gate, filter_taps, skip_gain):
    own_rows, channels = in_gate.shape
    copies = lax.axis_size("grp")
    core = lax.axis_index("grp") % 2
    half = own_rows // 2
    payload = prologue(core.astype(jnp.int32), in_gate, values, filter_taps)
    spread = lax.all_to_all(payload, "seq", split_axis=0, concat_axis=1, tiled=True)
    ch = spread.shape[0]
    spread = spread.reshape(ch, -1, own_rows + half)
    gated_spread = spread[:, :, :own_rows].reshape(ch, -1)
    mine = spread[:, :, own_rows:]
    theirs = lax.ppermute(mine, "grp", [(g, g ^ 1) for g in range(copies)])
    first = jnp.where(core == 0, mine, theirs)
    second = jnp.where(core == 0, theirs, mine)
    taps_full = jnp.stack([first, second], axis=2).reshape(ch, -1)
    conv = fused_conv(gated_spread, taps_full)
    back = lax.all_to_all(conv, "seq", split_axis=1, concat_axis=0, tiled=True)
    gated = in_gate.astype(jnp.float32) * values.astype(jnp.float32)
    total = back.T + skip_gain[None, :] * gated
    return (out_gate.astype(jnp.float32) * total).astype(jnp.bfloat16)


def solution(mesh):
    in_specs = (
        P(("grp", "seq"), None),
        P(("grp", "seq"), None),
        P(("grp", "seq"), None),
        P("seq", None),
        P(),
    )
    out_specs = P(("grp", "seq"), None)
    return jax.shard_map(local, mesh=mesh, in_specs=in_specs, out_specs=out_specs, check_vma=False)
```

```python
import jax
import jax.numpy as jnp
from jax import lax
from jax.experimental import pallas as pl
from jax.experimental.pallas import tpu as pltpu
from jax.sharding import PartitionSpec as P

exact_mode = lax.Precision.HIGH
SIDE = 128


def angle_table(rows, cols, period):
    product = jnp.arange(rows, dtype=jnp.int32)[:, None] * jnp.arange(cols, dtype=jnp.int32)[None, :]
    return (product % period).astype(jnp.float32) * (2.0 * jnp.pi / period)


def dft_tables(filled):
    rows = SIDE // 2 + 8
    first = angle_table(rows, filled, SIDE)
    stage_a = jnp.concatenate([jnp.cos(first), -jnp.sin(first)], axis=0)
    second = angle_table(SIDE, SIDE, SIDE)
    cos_b, sin_b = jnp.cos(second), jnp.sin(second)
    forward_b = jnp.block([[cos_b, -sin_b], [sin_b, cos_b]])
    inverse_b = jnp.block([[cos_b, sin_b], [-sin_b, cos_b]])
    twist = angle_table(rows, SIDE, SIDE * SIDE)
    row = jnp.arange(rows, dtype=jnp.int32)
    weight = jnp.where((row == 0) | (row == SIDE // 2), 1.0, jnp.where(row < SIDE // 2, 2.0, 0.0))
    stage_inv = stage_a * (jnp.concatenate([weight, weight])[:, None] / (SIDE * SIDE))
    return stage_a, forward_b, inverse_b, jnp.cos(twist), jnp.sin(twist), stage_inv


def spectrum(signal, tables):
    stage_a, forward_b, _, twist_cos, twist_sin, _ = tables
    rows = twist_cos.shape[0]
    ch, n = signal.shape
    x = signal.reshape(ch, n // SIDE, SIDE)
    a = jnp.einsum("kn,bnm->bkm", stage_a, x, precision=exact_mode)
    a_re, a_im = a[:, :rows], a[:, rows:]
    b_re = a_re * twist_cos + a_im * twist_sin
    b_im = a_im * twist_cos - a_re * twist_sin
    return jnp.einsum(
        "bkm,mj->bkj", jnp.concatenate([b_re, b_im], axis=-1), forward_b, precision=exact_mode
    )


def inverse_prefix(spec_g, spec_h, tables, n):
    _, _, inverse_b, twist_cos, twist_sin, stage_inv = tables
    g_re, g_im = spec_g[..., :SIDE], spec_g[..., SIDE:]
    h_re, h_im = spec_h[..., :SIDE], spec_h[..., SIDE:]
    prod = jnp.concatenate([g_re * h_re - g_im * h_im, g_re * h_im + g_im * h_re], axis=-1)
    q = jnp.einsum("bkj,jm->bkm", prod, inverse_b, precision=exact_mode)
    q_re, q_im = q[..., :SIDE], q[..., SIDE:]
    r_re = q_re * twist_cos - q_im * twist_sin
    r_im = q_im * twist_cos + q_re * twist_sin
    y = jnp.einsum(
        "kn,bkm->bnm", stage_inv, jnp.concatenate([r_re, r_im], axis=1), precision=exact_mode
    )
    return y.reshape(y.shape[0], n)


def prologue_kernel(core_ref, gate_ref, values_ref, taps_ref, out_ref):
    step = pl.program_id(0)
    gated_steps = pl.num_programs(0) - 1

    rows = gate_ref.shape[0]
    eye = (
        lax.broadcasted_iota(jnp.int32, (rows, rows), 0)
        == lax.broadcasted_iota(jnp.int32, (rows, rows), 1)
    ).astype(jnp.bfloat16)
    dims = (((0,), (0,)), ((), ()))

    def flip(x):
        return lax.dot_general(x, eye, dims, preferred_element_type=jnp.float32)

    @pl.when(step < gated_steps)
    def _():
        gated = gate_ref[...].astype(jnp.float32) * values_ref[...].astype(jnp.float32)
        high = gated.astype(jnp.bfloat16)
        low = (gated - high.astype(jnp.float32)).astype(jnp.bfloat16)
        out_ref[...] = flip(high) + flip(low)

    @pl.when(step == gated_steps)
    def _():
        out_ref[...] = flip(taps_ref[...])


def prologue(core, in_gate, values, filter_taps):
    rows, channels = in_gate.shape
    half = rows // 2
    gated_steps = rows // half
    last = gated_steps - 1
    row_block = pl.BlockSpec((half, channels), lambda j, c: (jnp.minimum(j, last), 0))
    taps_block = pl.BlockSpec((half, channels), lambda j, c: (c[0], 0))
    grid_spec = pltpu.PrefetchScalarGridSpec(
        num_scalar_prefetch=1,
        grid=(gated_steps + 1,),
        in_specs=[row_block, row_block, taps_block],
        out_specs=pl.BlockSpec((channels, half), lambda j, c: (0, j)),
    )
    return pl.pallas_call(
        prologue_kernel,
        grid_spec=grid_spec,
        out_shape=jax.ShapeDtypeStruct((channels, rows + half), jnp.float32),
    )(core.reshape(1), in_gate, values, filter_taps)


def local(in_gate, values, out_gate, filter_taps, skip_gain):
    own_rows, channels = in_gate.shape
    copies = lax.axis_size("grp")
    core = lax.axis_index("grp") % 2
    half = own_rows // 2
    payload = prologue(core.astype(jnp.int32), in_gate, values, filter_taps)
    spread = lax.all_to_all(payload, "seq", split_axis=0, concat_axis=1, tiled=True)
    ch = spread.shape[0]
    spread = spread.reshape(ch, -1, own_rows + half)
    gated_spread = spread[:, :, :own_rows].reshape(ch, -1)
    mine = spread[:, :, own_rows:]
    theirs = lax.ppermute(mine, "grp", [(g, g ^ 1) for g in range(copies)])
    n = gated_spread.shape[1]
    tables = dft_tables(n // SIDE)
    spec_g = spectrum(gated_spread, tables)
    first = jnp.where(core == 0, mine, theirs)
    second = jnp.where(core == 0, theirs, mine)
    taps_full = jnp.stack([first, second], axis=2).reshape(ch, -1)
    spec_h = spectrum(taps_full, tables)
    conv = inverse_prefix(spec_g, spec_h, tables, n)
    back = lax.all_to_all(conv, "seq", split_axis=1, concat_axis=0, tiled=True)
    gated = in_gate.astype(jnp.float32) * values.astype(jnp.float32)
    total = back.T + skip_gain[None, :] * gated
    return (out_gate.astype(jnp.float32) * total).astype(jnp.bfloat16)


def solution(mesh):
    in_specs = (
        P(("grp", "seq"), None),
        P(("grp", "seq"), None),
        P(("grp", "seq"), None),
        P("seq", None),
        P(),
    )
    out_specs = P(("grp", "seq"), None)
    return jax.shard_map(local, mesh=mesh, in_specs=in_specs, out_specs=out_specs, check_vma=False)
```

```python
import jax
import jax.numpy as jnp
from jax import lax
from jax.experimental import pallas as pl
from jax.experimental.pallas import tpu as pltpu
from jax.sharding import PartitionSpec as P

exact_mode = lax.Precision.HIGH
SIDE = 128


def angle_table(rows, cols, period):
    product = jnp.arange(rows, dtype=jnp.int32)[:, None] * jnp.arange(cols, dtype=jnp.int32)[None, :]
    return (product % period).astype(jnp.float32) * (2.0 * jnp.pi / period)


def dft_tables(filled):
    rows = SIDE // 2 + 8
    first = angle_table(rows, filled, SIDE)
    stage_a = jnp.concatenate([jnp.cos(first), -jnp.sin(first)], axis=0)
    second = angle_table(SIDE, SIDE, SIDE)
    cos_b, sin_b = jnp.cos(second), jnp.sin(second)
    forward_b = jnp.block([[cos_b, -sin_b], [sin_b, cos_b]])
    inverse_b = jnp.block([[cos_b, sin_b], [-sin_b, cos_b]])
    twist = angle_table(rows, SIDE, SIDE * SIDE)
    row = jnp.arange(rows, dtype=jnp.int32)
    weight = jnp.where((row == 0) | (row == SIDE // 2), 1.0, jnp.where(row < SIDE // 2, 2.0, 0.0))
    stage_inv = stage_a * jnp.concatenate([weight, weight])[:, None]
    return stage_a, forward_b, inverse_b, jnp.cos(twist), jnp.sin(twist), stage_inv


def spectrum(signal, tables):
    stage_a, forward_b, _, twist_cos, twist_sin, _ = tables
    rows = twist_cos.shape[0]
    ch, n = signal.shape
    x = signal.reshape(ch, n // SIDE, SIDE)
    a = jnp.einsum("kn,bnm->bkm", stage_a, x, precision=exact_mode)
    a_re, a_im = a[:, :rows], a[:, rows:]
    b_re = a_re * twist_cos + a_im * twist_sin
    b_im = a_im * twist_cos - a_re * twist_sin
    return jnp.einsum(
        "bkm,mj->bkj", jnp.concatenate([b_re, b_im], axis=-1), forward_b, precision=exact_mode
    )


def inverse_prefix(spec_g, spec_h, tables, n):
    _, _, inverse_b, twist_cos, twist_sin, stage_inv = tables
    g_re, g_im = spec_g[..., :SIDE], spec_g[..., SIDE:]
    h_re, h_im = spec_h[..., :SIDE], spec_h[..., SIDE:]
    prod = jnp.concatenate([g_re * h_re - g_im * h_im, g_re * h_im + g_im * h_re], axis=-1)
    q = jnp.einsum("bkj,jm->bkm", prod, inverse_b, precision=exact_mode)
    q_re, q_im = q[..., :SIDE], q[..., SIDE:]
    r_re = q_re * twist_cos - q_im * twist_sin
    r_im = q_im * twist_cos + q_re * twist_sin
    y = jnp.einsum(
        "kn,bkm->bnm", stage_inv, jnp.concatenate([r_re, r_im], axis=1), precision=exact_mode
    )
    return y.reshape(y.shape[0], n) * (1.0 / (SIDE * SIDE))


def prologue_kernel(gate_ref, values_ref, out_ref):
    gated = gate_ref[...].astype(jnp.float32) * values_ref[...].astype(jnp.float32)
    out_ref[...] = gated.T


def prologue(in_gate, values):
    rows, channels = in_gate.shape
    block = rows // 2
    return pl.pallas_call(
        prologue_kernel,
        grid=(rows // block,),
        in_specs=[pl.BlockSpec((block, channels), lambda j: (j, 0))] * 2,
        out_specs=pl.BlockSpec((channels, block), lambda j: (0, j)),
        out_shape=jax.ShapeDtypeStruct((channels, rows), jnp.float32),
    )(in_gate, values)


def local(in_gate, values, out_gate, filter_taps, skip_gain):
    own_rows, channels = in_gate.shape
    copies = lax.axis_size("grp")
    groups = lax.axis_size("seq")
    ch = channels // groups
    quarter = lax.axis_index("grp") % 4
    share = ch // 4
    gated_t = prologue(in_gate, values).reshape(groups, ch, own_rows)
    taps = filter_taps.astype(jnp.float32).reshape(own_rows, groups, 4, share)
    taps_part = lax.dynamic_index_in_dim(taps, quarter, axis=2, keepdims=False)
    payload = jnp.concatenate([gated_t, jnp.transpose(taps_part, (1, 2, 0))], axis=1)
    spread = lax.all_to_all(payload, "seq", split_axis=0, concat_axis=0, tiled=True)
    gated_spread = jnp.transpose(spread[:, :ch], (1, 0, 2)).reshape(ch, -1)
    mine = jnp.transpose(spread[:, ch:], (1, 0, 2)).reshape(share, -1)
    across = lax.ppermute(mine, "grp", [(g, g ^ 2) for g in range(copies)])
    pair = lax.ppermute(jnp.stack([mine, across]), "grp", [(g, g ^ 1) for g in range(copies)])
    n = gated_spread.shape[1]
    tables = dft_tables(n // SIDE)
    spec_g = spectrum(gated_spread, tables)
    pieces = []
    for j in range(4):
        t = quarter ^ j
        pieces.append(
            jnp.where(t == 0, mine, jnp.where(t == 2, across, jnp.where(t == 1, pair[0], pair[1])))
        )
    taps_full = jnp.concatenate(pieces, axis=0)
    spec_h = spectrum(taps_full, tables)
    conv = inverse_prefix(spec_g, spec_h, tables, n)
    back = lax.all_to_all(conv, "seq", split_axis=1, concat_axis=0, tiled=True)
    gated = in_gate.astype(jnp.float32) * values.astype(jnp.float32)
    total = back.T + skip_gain[None, :] * gated
    return (out_gate.astype(jnp.float32) * total).astype(jnp.bfloat16)


def solution(mesh):
    in_specs = (
        P(("grp", "seq"), None),
        P(("grp", "seq"), None),
        P(("grp", "seq"), None),
        P("seq", None),
        P(),
    )
    out_specs = P(("grp", "seq"), None)
    return jax.shard_map(local, mesh=mesh, in_specs=in_specs, out_specs=out_specs, check_vma=False)
```

```python
import jax
import jax.numpy as jnp
from jax import lax
from jax.experimental import pallas as pl
from jax.experimental.pallas import tpu as pltpu
from jax.sharding import PartitionSpec as P

exact_mode = lax.Precision.HIGH
SIDE = 128


def angle_table(rows, cols, period):
    product = jnp.arange(rows, dtype=jnp.int32)[:, None] * jnp.arange(cols, dtype=jnp.int32)[None, :]
    return (product % period).astype(jnp.float32) * (2.0 * jnp.pi / period)


def dft_tables(filled):
    rows = SIDE // 2 + 8
    first = angle_table(rows, filled, SIDE)
    stage_a = jnp.concatenate([jnp.cos(first), -jnp.sin(first)], axis=0)
    second = angle_table(SIDE, SIDE, SIDE)
    cos_b, sin_b = jnp.cos(second), jnp.sin(second)
    forward_b = jnp.block([[cos_b, -sin_b], [sin_b, cos_b]])
    inverse_b = jnp.block([[cos_b, sin_b], [-sin_b, cos_b]])
    twist = angle_table(rows, SIDE, SIDE * SIDE)
    row = jnp.arange(rows, dtype=jnp.int32)
    weight = jnp.where((row == 0) | (row == SIDE // 2), 1.0, jnp.where(row < SIDE // 2, 2.0, 0.0))
    stage_inv = stage_a * jnp.concatenate([weight, weight])[:, None]
    return stage_a, forward_b, inverse_b, jnp.cos(twist), jnp.sin(twist), stage_inv


def spectrum(signal, tables):
    stage_a, forward_b, _, twist_cos, twist_sin, _ = tables
    rows = twist_cos.shape[0]
    ch, n = signal.shape
    x = signal.reshape(ch, n // SIDE, SIDE)
    a = jnp.einsum("kn,bnm->bkm", stage_a, x, precision=exact_mode)
    a_re, a_im = a[:, :rows], a[:, rows:]
    b_re = a_re * twist_cos + a_im * twist_sin
    b_im = a_im * twist_cos - a_re * twist_sin
    return jnp.einsum(
        "bkm,mj->bkj", jnp.concatenate([b_re, b_im], axis=-1), forward_b, precision=exact_mode
    )


def inverse_prefix(spec_g, spec_h, tables, n):
    _, _, inverse_b, twist_cos, twist_sin, stage_inv = tables
    g_re, g_im = spec_g[..., :SIDE], spec_g[..., SIDE:]
    h_re, h_im = spec_h[..., :SIDE], spec_h[..., SIDE:]
    prod = jnp.concatenate([g_re * h_re - g_im * h_im, g_re * h_im + g_im * h_re], axis=-1)
    q = jnp.einsum("bkj,jm->bkm", prod, inverse_b, precision=exact_mode)
    q_re, q_im = q[..., :SIDE], q[..., SIDE:]
    r_re = q_re * twist_cos - q_im * twist_sin
    r_im = q_im * twist_cos + q_re * twist_sin
    y = jnp.einsum(
        "kn,bkm->bnm", stage_inv, jnp.concatenate([r_re, r_im], axis=1), precision=exact_mode
    )
    return y.reshape(y.shape[0], n) * (1.0 / (SIDE * SIDE))


def prologue_kernel(core_ref, gate_ref, values_ref, taps_ref, out_ref):
    step = pl.program_id(0)
    gated_steps = pl.num_programs(0) - 1

    @pl.when(step < gated_steps)
    def _():
        gated = gate_ref[...].astype(jnp.float32) * values_ref[...].astype(jnp.float32)
        out_ref[...] = gated.T

    @pl.when(step == gated_steps)
    def _():
        out_ref[...] = taps_ref[...].astype(jnp.float32).T


def prologue(core, in_gate, values, filter_taps):
    rows, channels = in_gate.shape
    half = rows // 2
    gated_steps = rows // half
    last = gated_steps - 1
    row_block = pl.BlockSpec((half, channels), lambda j, c: (jnp.minimum(j, last), 0))
    taps_block = pl.BlockSpec((half, channels), lambda j, c: (c[0], 0))
    grid_spec = pltpu.PrefetchScalarGridSpec(
        num_scalar_prefetch=1,
        grid=(gated_steps + 1,),
        in_specs=[row_block, row_block, taps_block],
        out_specs=pl.BlockSpec((channels, half), lambda j, c: (0, j)),
    )
    return pl.pallas_call(
        prologue_kernel,
        grid_spec=grid_spec,
        out_shape=jax.ShapeDtypeStruct((channels, rows + half), jnp.float32),
    )(core.reshape(1), in_gate, values, filter_taps)


def regroup_kernel(x_ref, out_ref):
    width = out_ref.shape[2]
    for d in range(out_ref.shape[0]):
        out_ref[d] = x_ref[:, d * width:(d + 1) * width]


def regroup(x, groups):
    ch, n = x.shape
    return pl.pallas_call(
        regroup_kernel,
        in_specs=[pl.BlockSpec(memory_space=pltpu.VMEM)],
        out_specs=pl.BlockSpec(memory_space=pltpu.VMEM),
        out_shape=jax.ShapeDtypeStruct((groups, ch, n // groups), x.dtype),
    )(x)


def local(in_gate, values, out_gate, filter_taps, skip_gain):
    own_rows, channels = in_gate.shape
    copies = lax.axis_size("grp")
    core = lax.axis_index("grp") % 2
    half = own_rows // 2
    payload = prologue(core.astype(jnp.int32), in_gate, values, filter_taps)
    spread = lax.all_to_all(payload, "seq", split_axis=0, concat_axis=1, tiled=True)
    ch = spread.shape[0]
    spread = spread.reshape(ch, -1, own_rows + half)
    gated_spread = spread[:, :, :own_rows].reshape(ch, -1)
    mine = spread[:, :, own_rows:]
    theirs = lax.ppermute(mine, "grp", [(g, g ^ 1) for g in range(copies)])
    n = gated_spread.shape[1]
    tables = dft_tables(n // SIDE)
    spec_g = spectrum(gated_spread, tables)
    first = jnp.where(core == 0, mine, theirs)
    second = jnp.where(core == 0, theirs, mine)
    taps_full = jnp.stack([first, second], axis=2).reshape(ch, -1)
    spec_h = spectrum(taps_full, tables)
    conv = inverse_prefix(spec_g, spec_h, tables, n)
    groups = lax.axis_size("seq")
    back = lax.all_to_all(regroup(conv, groups), "seq", split_axis=0, concat_axis=0, tiled=True)
    back = back.reshape(channels, own_rows)
    gated = in_gate.astype(jnp.float32) * values.astype(jnp.float32)
    total = back.T + skip_gain[None, :] * gated
    return (out_gate.astype(jnp.float32) * total).astype(jnp.bfloat16)


def solution(mesh):
    in_specs = (
        P(("grp", "seq"), None),
        P(("grp", "seq"), None),
        P(("grp", "seq"), None),
        P("seq", None),
        P(),
    )
    out_specs = P(("grp", "seq"), None)
    return jax.shard_map(local, mesh=mesh, in_specs=in_specs, out_specs=out_specs, check_vma=False)
```

```python
import jax
import jax.numpy as jnp
from jax import lax
from jax.experimental import pallas as pl
from jax.experimental.pallas import tpu as pltpu
from jax.sharding import PartitionSpec as P

exact_mode = lax.Precision.HIGH
SIDE = 128


def angle_table(rows, cols, period):
    product = jnp.arange(rows, dtype=jnp.int32)[:, None] * jnp.arange(cols, dtype=jnp.int32)[None, :]
    return (product % period).astype(jnp.float32) * (2.0 * jnp.pi / period)


def dft_tables(filled):
    rows = SIDE // 2 + 8
    first = angle_table(rows, filled, SIDE)
    stage_a = jnp.concatenate([jnp.cos(first), -jnp.sin(first)], axis=0)
    second = angle_table(SIDE, SIDE, SIDE)
    cos_b, sin_b = jnp.cos(second), jnp.sin(second)
    forward_b = jnp.block([[cos_b, -sin_b], [sin_b, cos_b]])
    inverse_b = jnp.block([[cos_b, sin_b], [-sin_b, cos_b]])
    twist = angle_table(rows, SIDE, SIDE * SIDE)
    row = jnp.arange(rows, dtype=jnp.int32)
    weight = jnp.where((row == 0) | (row == SIDE // 2), 1.0, jnp.where(row < SIDE // 2, 2.0, 0.0))
    stage_inv = stage_a * jnp.concatenate([weight, weight])[:, None]
    return stage_a, forward_b, inverse_b, jnp.cos(twist), jnp.sin(twist), stage_inv


def spectrum(signal, tables):
    stage_a, forward_b, _, twist_cos, twist_sin, _ = tables
    rows = twist_cos.shape[0]
    ch, n = signal.shape
    x = signal.reshape(ch, n // SIDE, SIDE)
    a = jnp.einsum("kn,bnm->bkm", stage_a, x, precision=exact_mode)
    a_re, a_im = a[:, :rows], a[:, rows:]
    b_re = a_re * twist_cos + a_im * twist_sin
    b_im = a_im * twist_cos - a_re * twist_sin
    return jnp.einsum(
        "bkm,mj->bkj", jnp.concatenate([b_re, b_im], axis=-1), forward_b, precision=exact_mode
    )


def inverse_prefix(spec_g, spec_h, tables, n):
    _, _, inverse_b, twist_cos, twist_sin, stage_inv = tables
    g_re, g_im = spec_g[..., :SIDE], spec_g[..., SIDE:]
    h_re, h_im = spec_h[..., :SIDE], spec_h[..., SIDE:]
    prod = jnp.concatenate([g_re * h_re - g_im * h_im, g_re * h_im + g_im * h_re], axis=-1)
    q = jnp.einsum("bkj,jm->bkm", prod, inverse_b, precision=exact_mode)
    q_re, q_im = q[..., :SIDE], q[..., SIDE:]
    r_re = q_re * twist_cos - q_im * twist_sin
    r_im = q_im * twist_cos + q_re * twist_sin
    y = jnp.einsum(
        "kn,bkm->bnm", stage_inv, jnp.concatenate([r_re, r_im], axis=1), precision=exact_mode
    )
    return y.reshape(y.shape[0], n) * (1.0 / (SIDE * SIDE))


def prologue_kernel(core_ref, gate_ref, values_ref, taps_ref, out_ref):
    step = pl.program_id(0)
    gated_steps = pl.num_programs(0) - 1

    @pl.when(step < gated_steps)
    def _():
        gated = gate_ref[...].astype(jnp.float32) * values_ref[...].astype(jnp.float32)
        out_ref[...] = gated.T

    @pl.when(step == gated_steps)
    def _():
        out_ref[...] = taps_ref[...].astype(jnp.float32).T


def prologue(core, in_gate, values, filter_taps):
    rows, channels = in_gate.shape
    half = rows // 2
    gated_steps = rows // half
    last = gated_steps - 1
    row_block = pl.BlockSpec((half, channels), lambda j, c: (jnp.minimum(j, last), 0))
    taps_block = pl.BlockSpec((half, channels), lambda j, c: (c[0], 0))
    grid_spec = pltpu.PrefetchScalarGridSpec(
        num_scalar_prefetch=1,
        grid=(gated_steps + 1,),
        in_specs=[row_block, row_block, taps_block],
        out_specs=pl.BlockSpec((channels, half), lambda j, c: (0, j)),
    )
    return pl.pallas_call(
        prologue_kernel,
        grid_spec=grid_spec,
        out_shape=jax.ShapeDtypeStruct((channels, rows + half), jnp.float32),
    )(core.reshape(1), in_gate, values, filter_taps)


def local_body(in_gate, values, out_gate, filter_taps, skip_gain):
    own_rows, _ = in_gate.shape
    copies = lax.axis_size("grp")
    core = lax.axis_index("grp") % 2
    half = own_rows // 2
    payload = prologue(core.astype(jnp.int32), in_gate, values, filter_taps)
    spread = lax.all_to_all(payload, "seq", split_axis=0, concat_axis=1, tiled=True)
    ch = spread.shape[0]
    spread = spread.reshape(ch, -1, own_rows + half)
    gated_spread = spread[:, :, :own_rows].reshape(ch, -1)
    mine = spread[:, :, own_rows:]
    theirs = lax.ppermute(mine, "grp", [(g, g ^ 1) for g in range(copies)])
    n = gated_spread.shape[1]
    tables = dft_tables(n // SIDE)
    spec_g = spectrum(gated_spread, lax.optimization_barrier(tables))
    first = jnp.where(core == 0, mine, theirs)
    second = jnp.where(core == 0, theirs, mine)
    taps_full = jnp.stack([first, second], axis=2).reshape(ch, -1)
    spec_h = spectrum(taps_full, tables)
    conv = inverse_prefix(spec_g, spec_h, tables, n)
    back = lax.all_to_all(conv, "seq", split_axis=1, concat_axis=0, tiled=True)
    gated = in_gate.astype(jnp.float32) * values.astype(jnp.float32)
    total = back.T + skip_gain[None, :] * gated
    return (out_gate.astype(jnp.float32) * total).astype(jnp.bfloat16)


def solution(mesh):
    in_specs = (
        P(("grp", "seq"), None),
        P(("grp", "seq"), None),
        P(("grp", "seq"), None),
        P("seq", None),
        P(),
    )
    out_specs = P(("grp", "seq"), None)
    return jax.shard_map(local_body, mesh=mesh, in_specs=in_specs, out_specs=out_specs, check_vma=False)
```

```python
import jax
import jax.numpy as jnp
from jax import lax
from jax.experimental import pallas as pl
from jax.experimental.pallas import tpu as pltpu
from jax.sharding import PartitionSpec as P

exact_mode = lax.Precision.HIGH
SIDE = 128


def angle_table(rows, cols, period):
    product = jnp.arange(rows, dtype=jnp.int32)[:, None] * jnp.arange(cols, dtype=jnp.int32)[None, :]
    return (product % period).astype(jnp.float32) * (2.0 * jnp.pi / period)


def dft_tables(filled):
    rows = SIDE // 2 + 8
    first = angle_table(rows, filled, SIDE)
    stage_a = jnp.concatenate([jnp.cos(first), -jnp.sin(first)], axis=0)
    second = angle_table(SIDE, SIDE, SIDE)
    cos_b, sin_b = jnp.cos(second), jnp.sin(second)
    forward_b = jnp.block([[cos_b, -sin_b], [sin_b, cos_b]])
    inverse_b = jnp.block([[cos_b, sin_b], [-sin_b, cos_b]])
    twist = angle_table(rows, SIDE, SIDE * SIDE)
    row = jnp.arange(rows, dtype=jnp.int32)
    weight = jnp.where((row == 0) | (row == SIDE // 2), 1.0, jnp.where(row < SIDE // 2, 2.0, 0.0))
    stage_inv = stage_a * jnp.concatenate([weight, weight])[:, None]
    return stage_a, forward_b, inverse_b, jnp.cos(twist), jnp.sin(twist), stage_inv


def spectrum(signal, tables):
    stage_a, forward_b, _, twist_cos, twist_sin, _ = tables
    rows = twist_cos.shape[0]
    ch, n = signal.shape
    x = signal.reshape(ch, n // SIDE, SIDE)
    a = jnp.einsum("kn,bnm->bkm", stage_a, x, precision=exact_mode)
    a_re, a_im = a[:, :rows], a[:, rows:]
    b_re = a_re * twist_cos + a_im * twist_sin
    b_im = a_im * twist_cos - a_re * twist_sin
    return jnp.einsum(
        "bkm,mj->bkj", jnp.concatenate([b_re, b_im], axis=-1), forward_b, precision=exact_mode
    )


def inverse_prefix(spec_g, spec_h, tables, n):
    _, _, inverse_b, twist_cos, twist_sin, stage_inv = tables
    g_re, g_im = spec_g[..., :SIDE], spec_g[..., SIDE:]
    h_re, h_im = spec_h[..., :SIDE], spec_h[..., SIDE:]
    prod = jnp.concatenate([g_re * h_re - g_im * h_im, g_re * h_im + g_im * h_re], axis=-1)
    q = jnp.einsum("bkj,jm->bkm", prod, inverse_b, precision=exact_mode)
    q_re, q_im = q[..., :SIDE], q[..., SIDE:]
    r_re = q_re * twist_cos - q_im * twist_sin
    r_im = q_im * twist_cos + q_re * twist_sin
    y = jnp.einsum(
        "kn,bkm->bnm", stage_inv, jnp.concatenate([r_re, r_im], axis=1), precision=exact_mode
    )
    return y.reshape(y.shape[0], n) * (1.0 / (SIDE * SIDE))


def prologue_kernel(core_ref, gate_ref, values_ref, taps_ref, out_ref):
    step = pl.program_id(0)
    gated_steps = pl.num_programs(0) - 1

    @pl.when(step < gated_steps)
    def _():
        gated = gate_ref[...].astype(jnp.float32) * values_ref[...].astype(jnp.float32)
        out_ref[...] = gated.T

    @pl.when(step == gated_steps)
    def _():
        out_ref[...] = taps_ref[...].astype(jnp.float32).T


def prologue(core, in_gate, values, filter_taps):
    rows, channels = in_gate.shape
    half = rows // 2
    gated_steps = rows // half
    last = gated_steps - 1
    row_block = pl.BlockSpec((half, channels), lambda j, c: (jnp.minimum(j, last), 0))
    taps_block = pl.BlockSpec((half, channels), lambda j, c: (c[0], 0))
    grid_spec = pltpu.PrefetchScalarGridSpec(
        num_scalar_prefetch=1,
        grid=(gated_steps + 1,),
        in_specs=[row_block, row_block, taps_block],
        out_specs=pl.BlockSpec((channels, half), lambda j, c: (0, j)),
    )
    return pl.pallas_call(
        prologue_kernel,
        grid_spec=grid_spec,
        out_shape=jax.ShapeDtypeStruct((channels, rows + half), jnp.float32),
    )(core.reshape(1), in_gate, values, filter_taps)


def local_body(in_gate, values, out_gate, filter_taps, skip_gain):
    own_rows, _ = in_gate.shape
    copies = lax.axis_size("grp")
    core = lax.axis_index("grp") % 2
    half = own_rows // 2
    payload = prologue(core.astype(jnp.int32), in_gate, values, filter_taps)
    spread = lax.all_to_all(payload, "seq", split_axis=0, concat_axis=1, tiled=True)
    ch = spread.shape[0]
    spread = spread.reshape(ch, -1, own_rows + half)
    gated_spread = spread[:, :, :own_rows].reshape(ch, -1)
    mine = spread[:, :, own_rows:]
    theirs = lax.ppermute(mine, "grp", [(g, g ^ 1) for g in range(copies)])
    n = gated_spread.shape[1]
    tables = dft_tables(n // SIDE)
    spec_g = spectrum(gated_spread, lax.optimization_barrier(tables))
    taps_full = jnp.stack([mine, theirs], axis=2).reshape(ch, -1)
    stage_a = tables[0]
    swapped = stage_a[:, jnp.arange(stage_a.shape[1]) ^ (half // SIDE)]
    spec_h = spectrum(taps_full, (jnp.where(core == 0, stage_a, swapped),) + tuple(tables[1:]))
    conv = inverse_prefix(spec_g, spec_h, tables, n)
    back = lax.all_to_all(conv, "seq", split_axis=1, concat_axis=0, tiled=True)
    gated = in_gate.astype(jnp.float32) * values.astype(jnp.float32)
    total = back.T + skip_gain[None, :] * gated
    return (out_gate.astype(jnp.float32) * total).astype(jnp.bfloat16)


def solution(mesh):
    in_specs = (
        P(("grp", "seq"), None),
        P(("grp", "seq"), None),
        P(("grp", "seq"), None),
        P("seq", None),
        P(),
    )
    out_specs = P(("grp", "seq"), None)
    return jax.shard_map(local_body, mesh=mesh, in_specs=in_specs, out_specs=out_specs, check_vma=False)
```
